32 devices in a mesh: grp: 2 (over y), cell: 8 (over z, x), gene: 2 (over core).
Axes of the slice: x: 2, y: 2, z: 4, core: 2. Of those that a mesh axis runs over, the one named last changes fastest.
Arguments:
- expression: bfloat16 [2048, 16384], P(('grp', 'cell'), 'gene'), parts along dimension 0, may hold values from -6 to 6
- design: bfloat16 [2048, 128], P(('grp', 'cell')), parts along dimension 0, may hold values from -24 to 24
- quantile_level: float32 [16384], P('gene'), may hold values from 0.1 to 0.9
Outputs:
- quantile_slack: bfloat16 [2048, 16384], P(('grp', 'cell'), 'gene'), parts along dimension 0
- low_rank_coef: float32 [32768, 128], P(('grp', 'gene', 'cell')), parts along dimension 0
The draws below stay inside these ranges and needn't reach their ends.
There are 2 independent parts, one for each index of `grp`. The reference program is written for one: setup_inputs(seed, part) draws one part's arguments, and reference() takes and returns one part's arrays. A program takes and returns all parts, laid end to end along the dimension named above; an argument that names none is the same for every part. Nothing has to cross between parts.
All inputs are finite; a program needn't handle non-finite values.
Results may differ from the reference program's by a relative error of at most 0.0025.
The reference program's roundings to bfloat16 on the way (of `coef_low`) count: a program that leaves them out, or rounds other values in their place, can miss the bound.
Values may be sent and summed in bfloat16 or wider, within the bound.
No kernel may reach another device: no remote copies, remote signals or barrier semaphores. Data moves between devices by JAX's collectives and lax.ppermute only.
A program may use at most 64 MiB of HBM per device.

```python
import math
import jax
import jax.numpy as jnp
from jax import lax

P_SIZE = 128
Q = 16384
NS_STEPS = 8
NCELLS = 1024


def draw_design(key, part):
    key_col, key_base = jax.random.split(key, 2)
    col_scale = jnp.exp(jax.random.uniform(key_col, (1, P_SIZE), jnp.float32, 0.0, math.log(30.0)))
    base = jnp.clip(jax.random.normal(key_base, (NCELLS, P_SIZE), jnp.float32), -4.0, 4.0)
    values = base * col_scale / math.sqrt(NCELLS)
    return values.astype(jnp.bfloat16)


def spiked(result, stream_key, source, target, blocks, factor):
    owner, partner = [(jnp.arange(result.shape[axis_at]) // (result.shape[axis_at] // blocks)).reshape([-1 if axis == axis_at else 1 for axis in range(result.ndim)]) for axis_at in (source, target)]
    chosen = jax.random.permutation(stream_key, blocks)[partner]
    strong = (owner == chosen) | (owner == (partner + blocks // 2) % blocks)
    return jnp.where(strong, factor * result, result)


def block_scale(key, dims, shards, least, high):
    factor_of, own = 1.0, jax.random.fold_in(key, 6)
    for axis_at, parts in shards:
        draws = jnp.exp(jax.random.uniform(jax.random.fold_in(own, axis_at), (parts,), jnp.float32, least / len(shards), high / len(shards)))
        factor_of = factor_of * jnp.repeat(draws, dims[axis_at] // parts).reshape([-1 if axis == axis_at else 1 for axis in range(len(dims))])
    return factor_of


def heavy_noise(key, dims, spread, reach, cuts, heavy, held_as=jnp.bfloat16):
    entries = spread * jax.random.normal(key, dims, jnp.float32)
    if cuts:
        entries = entries * block_scale(key, dims, cuts, -0.22, 0.18)
    return jnp.clip(spiked(entries, jax.random.fold_in(key, 3), *heavy), -reach, reach).astype(held_as)


def setup_inputs(seed: int = 0, part: int = 0) -> dict:
    arg_keys = jax.random.split(jax.random.key(seed), 4)
    part_splits = jax.random.split(jax.random.fold_in(arg_keys[3], part), 4)
    expression = heavy_noise(part_splits[0], (NCELLS, Q), 1.0, 6.0, ((0, 8), (1, 2)), (0, 1, 8, 2.0))
    design = draw_design(jax.random.fold_in(jax.random.fold_in(arg_keys[3], part), 71), part)
    quantile_level = jnp.clip(0.1 + 0.79999997 * jax.random.uniform(arg_keys[2], (Q,), jnp.float32) ** block_scale(arg_keys[2], (Q,), ((0, 2),), -0.2, 0.2), 0.1, 0.9)
    return {"expression": expression, "design": design, "quantile_level": quantile_level}


shrink_rate = 0.25

def matmul(left, right):
    return jnp.dot(left, right, precision=lax.Precision.HIGHEST)

def invert(matrix):
    identity = jnp.eye(matrix.shape[0], dtype=jnp.float32)
    factor = jnp.linalg.cholesky(matrix)
    lower_inv = lax.linalg.triangular_solve(factor, identity, left_side=True, lower=True)
    return matmul(lower_inv.T, lower_inv)

def newton(moment):
    identity = jnp.eye(moment.shape[0], dtype=jnp.float32)
    current = moment / jnp.trace(moment)
    root_inv = identity
    for sweep in range(NS_STEPS):
        middle = 1.5 * identity - 0.5 * matmul(root_inv, current)
        current = matmul(current, middle)
        root_inv = matmul(middle, root_inv)
    return root_inv

def reference(expression, design, quantile_level):
    identity = jnp.eye(P_SIZE, dtype=jnp.float32)
    gram_matrix = lax.dot_general(design.astype(jnp.float32), design.astype(jnp.float32), (((0,), (0,)), ((), ())), preferred_element_type=jnp.float32) + identity
    inverse = invert(gram_matrix)
    crossed = lax.dot_general(expression.astype(jnp.float32), design.astype(jnp.float32), (((0,), (0,)), ((), ())), preferred_element_type=jnp.float32)
    coef = matmul(crossed, inverse)
    moment = lax.dot_general(coef, coef, (((0,), (0,)), ((), ())), precision=lax.Precision.HIGHEST)
    root_inv = newton(moment)
    low_rank_coef = coef - shrink_rate / P_SIZE ** 0.5 * matmul(coef, root_inv)
    coef_low = coef.astype(jnp.bfloat16)
    block_width = min(Q, 2048)
    pieces = []
    for begin in range(0, Q, block_width):
        part_coef = coef_low[begin:begin + block_width]
        fitted = lax.dot_general(design.astype(jnp.float32), part_coef.astype(jnp.float32), (((1,), (1,)), ((), ())), preferred_element_type=jnp.float32)
        slack = expression[:, begin:begin + block_width].astype(jnp.float32) - fitted
        level = quantile_level[begin:begin + block_width][None, :]
        pieces.append((slack - jnp.clip(slack, level - 1.0, level)).astype(jnp.bfloat16))
    quantile_slack = jnp.concatenate(pieces, axis=1)
    return (quantile_slack, low_rank_coef)
```

```python
import math

import jax
import jax.numpy as jnp
from jax import lax
from jax.sharding import PartitionSpec as P

NS_STEPS = 8


shrink_rate = 0.25


def matmul(left, right):
    return jnp.dot(left, right, precision=lax.Precision.HIGHEST)


def invert(matrix):
    identity = jnp.eye(matrix.shape[0], dtype=jnp.float32)
    factor = jnp.linalg.cholesky(matrix)
    lower_inv = lax.linalg.triangular_solve(factor, identity, left_side=True, lower=True)
    return matmul(lower_inv.T, lower_inv)


def newton(moment):
    identity = jnp.eye(moment.shape[0], dtype=jnp.float32)
    current = moment / jnp.trace(moment)
    root_inv = identity
    for sweep in range(NS_STEPS):
        middle = 1.5 * identity - 0.5 * matmul(root_inv, current)
        current = matmul(current, middle)
        root_inv = matmul(middle, root_inv)
    return root_inv


def gather_rows(block, axis):
    n = lax.axis_size(axis)
    tiled = jnp.concatenate([block] * n, axis=0)
    return lax.all_to_all(tiled, axis, 0, 0, tiled=True)


def butterfly_sum(value, axis):
    n = lax.axis_size(axis)
    if n & (n - 1):
        return lax.psum(value, axis)
    bit = 1
    while bit < n:
        pairs = [(i, i ^ bit) for i in range(n)]
        value = value + lax.ppermute(value, axis, pairs)
        bit *= 2
    return value


def per_device(expression, design, quantile_level):
    width = design.shape[1]
    identity = jnp.eye(width, dtype=jnp.float32)
    design_all = gather_rows(design, "cell")
    gram_total = lax.dot_general(
        design_all, design_all, (((0,), (0,)), ((), ())), preferred_element_type=jnp.float32
    )
    inverse = invert(gram_total + identity)
    expression_genes = lax.all_to_all(expression, "cell", 1, 0, tiled=True)
    crossed = lax.dot_general(
        expression_genes, design_all, (((0,), (0,)), ((), ())), preferred_element_type=jnp.float32
    )
    coef = matmul(crossed, inverse)
    local_moment = lax.dot_general(
        coef, coef, (((0,), (0,)), ((), ())), precision=lax.Precision.HIGHEST
    )
    moment = butterfly_sum(butterfly_sum(local_moment, "gene"), "cell")
    root_inv = newton(moment)
    low_rank_coef = coef - shrink_rate / math.sqrt(width) * matmul(coef, root_inv)
    coef_low = coef.astype(jnp.bfloat16)
    fitted = lax.dot_general(
        design,
        gather_rows(coef_low, "cell"),
        (((1,), (1,)), ((), ())),
        preferred_element_type=jnp.float32,
    )
    slack = expression.astype(jnp.float32) - fitted
    level = quantile_level[None, :]
    quantile_slack = (slack - jnp.clip(slack, level - 1.0, level)).astype(jnp.bfloat16)
    return (quantile_slack, low_rank_coef)


def solution(mesh):
    placed = (P(("grp", "cell"), "gene"), P(("grp", "cell"), None), P("gene"))
    return jax.shard_map(
        per_device,
        mesh=mesh,
        in_specs=placed,
        out_specs=(P(("grp", "cell"), "gene"), P(("grp", "gene", "cell"), None)),
        check_vma=False,
    )
```

```python
import functools
import math

import jax
import jax.numpy as jnp
from jax import lax
from jax.sharding import PartitionSpec as P

NS_STEPS = 8


shrink_rate = 0.25


def matmul(left, right):
    return jnp.dot(left, right, precision=lax.Precision.HIGHEST)


def invert(matrix):
    identity = jnp.eye(matrix.shape[0], dtype=jnp.float32)
    factor = jnp.linalg.cholesky(matrix)
    lower_inv = lax.linalg.triangular_solve(factor, identity, left_side=True, lower=True)
    return matmul(lower_inv.T, lower_inv)


def newton(moment):
    identity = jnp.eye(moment.shape[0], dtype=jnp.float32)
    current = moment / jnp.trace(moment)
    root_inv = identity
    for sweep in range(NS_STEPS):
        middle = 1.5 * identity - 0.5 * matmul(root_inv, current)
        current = matmul(current, middle)
        root_inv = matmul(middle, root_inv)
    return root_inv


def cell_ring(mesh):
    devices = mesh.devices
    names = list(mesh.axis_names)
    index = [0] * len(names)
    index[names.index("cell")] = slice(None)
    line = list(devices[tuple(index)].reshape(-1))
    n = len(line)
    try:
        coords = [tuple(d.coords) for d in line]
    except (AttributeError, TypeError):
        return list(range(n))
    varying = [a for a in range(len(coords[0])) if len({c[a] for c in coords}) > 1]
    where = {c: i for i, c in enumerate(coords)}
    if len(varying) == 1:
        return sorted(range(n), key=lambda i: coords[i][varying[0]])
    if len(varying) != 2:
        return list(range(n))
    sizes = [len({c[a] for c in coords}) for a in varying]
    if sizes[0] * sizes[1] != n:
        return list(range(n))
    if sizes[0] % 2:
        varying, sizes = varying[::-1], sizes[::-1]
        if sizes[0] % 2:
            return list(range(n))
    lows = [min(c[a] for c in coords) for a in varying]
    path = []
    for u in range(sizes[0]):
        span = range(1, sizes[1]) if u % 2 == 0 else range(sizes[1] - 1, 0, -1)
        path += [(u, v) for v in span]
    path += [(u, 0) for u in range(sizes[0] - 1, -1, -1)]
    order = []
    for u, v in path:
        key = list(coords[0])
        key[varying[0]] = lows[0] + u
        key[varying[1]] = lows[1] + v
        order.append(where[tuple(key)])
    return order


def gather_rows(block, axis):
    n = lax.axis_size(axis)
    if n & (n - 1):
        return lax.all_gather(block, axis, axis=0, tiled=True)
    me = lax.axis_index(axis)
    bit = 1
    while bit < n:
        pairs = [(i, i ^ bit) for i in range(n)]
        other = lax.ppermute(block, axis, pairs)
        low = (me & bit) == 0
        block = jnp.where(low, jnp.concatenate([block, other]), jnp.concatenate([other, block]))
        bit *= 2
    return block


def butterfly_sum(value, axis):
    n = lax.axis_size(axis)
    if n & (n - 1):
        return lax.psum(value, axis)
    bit = 1
    while bit < n:
        pairs = [(i, i ^ bit) for i in range(n)]
        value = value + lax.ppermute(value, axis, pairs)
        bit *= 2
    return value


def per_device(ring, expression, design, quantile_level):
    n = len(ring)
    width = design.shape[1]
    span = expression.shape[1] // n
    identity = jnp.eye(width, dtype=jnp.float32)
    expression_genes = lax.all_to_all(expression, "cell", 1, 0, tiled=True)
    design_all = gather_rows(design, "cell")
    gram_total = lax.dot_general(
        design_all, design_all, (((0,), (0,)), ((), ())), preferred_element_type=jnp.float32
    )
    inverse = invert(gram_total + identity)
    crossed = lax.dot_general(
        expression_genes, design_all, (((0,), (0,)), ((), ())), preferred_element_type=jnp.float32
    )
    coef = matmul(crossed, inverse)
    local_moment = lax.dot_general(
        coef, coef, (((0,), (0,)), ((), ())), precision=lax.Precision.HIGHEST
    )
    moment = butterfly_sum(butterfly_sum(local_moment, "gene"), "cell")
    root_inv = newton(moment)
    low_rank_coef = coef - shrink_rate / math.sqrt(width) * matmul(coef, root_inv)
    coef_low_t = coef.astype(jnp.bfloat16).T

    ring_arr = jnp.array(ring, dtype=jnp.int32)
    pos_arr = jnp.array([ring.index(i) for i in range(n)], dtype=jnp.int32)
    me = lax.axis_index("cell")
    pos = pos_arr[me]
    forward = [(ring[q], ring[(q + 1) % n]) for q in range(n)]
    backward = [(ring[(q + 1) % n], ring[q]) for q in range(n)]

    out = jnp.zeros(expression.shape, jnp.bfloat16)

    def place(out, block, owner):
        start = owner * span
        fitted = jnp.dot(design, block, preferred_element_type=jnp.float32)
        local = lax.dynamic_slice_in_dim(expression, start, span, axis=1).astype(jnp.float32)
        level = lax.dynamic_slice_in_dim(quantile_level, start, span)[None, :]
        slack = local - fitted
        piece = (slack - jnp.clip(slack, level - 1.0, level)).astype(jnp.bfloat16)
        return lax.dynamic_update_slice_in_dim(out, piece, start, axis=1)

    out = place(out, coef_low_t, me)
    ahead, behind = coef_low_t, coef_low_t
    for step in range(1, n // 2 + 1):
        ahead = lax.ppermute(ahead, "cell", forward)
        out = place(out, ahead, ring_arr[(pos - step) % n])
        if step <= (n - 1) // 2:
            behind = lax.ppermute(behind, "cell", backward)
            out = place(out, behind, ring_arr[(pos + step) % n])
    return (out, low_rank_coef)


def solution(mesh):
    placed = (P(("grp", "cell"), "gene"), P(("grp", "cell"), None), P("gene"))
    ring = cell_ring(mesh)
    return jax.shard_map(
        functools.partial(per_device, ring),
        mesh=mesh,
        in_specs=placed,
        out_specs=(P(("grp", "cell"), "gene"), P(("grp", "gene", "cell"), None)),
        check_vma=False,
    )
```

```python
import functools
import math

import jax
import jax.numpy as jnp
from jax import lax
from jax.sharding import PartitionSpec as P

NS_STEPS = 8


shrink_rate = 0.25


def matmul(left, right):
    return jnp.dot(left, right, precision=lax.Precision.HIGHEST)


def invert(matrix):
    identity = jnp.eye(matrix.shape[0], dtype=jnp.float32)
    factor = jnp.linalg.cholesky(matrix)
    lower_inv = lax.linalg.triangular_solve(factor, identity, left_side=True, lower=True)
    return matmul(lower_inv.T, lower_inv)


def newton(moment):
    identity = jnp.eye(moment.shape[0], dtype=jnp.float32)
    current = moment / jnp.trace(moment)
    root_inv = identity
    for sweep in range(NS_STEPS):
        middle = 1.5 * identity - 0.5 * matmul(root_inv, current)
        current = matmul(current, middle)
        root_inv = matmul(middle, root_inv)
    return root_inv


def cell_ring(mesh):
    devices = mesh.devices
    names = list(mesh.axis_names)
    index = [0] * len(names)
    index[names.index("cell")] = slice(None)
    line = list(devices[tuple(index)].reshape(-1))
    n = len(line)
    try:
        coords = [tuple(d.coords) for d in line]
    except (AttributeError, TypeError):
        return list(range(n))
    varying = [a for a in range(len(coords[0])) if len({c[a] for c in coords}) > 1]
    where = {c: i for i, c in enumerate(coords)}
    if len(varying) == 1:
        return sorted(range(n), key=lambda i: coords[i][varying[0]])
    if len(varying) != 2:
        return list(range(n))
    sizes = [len({c[a] for c in coords}) for a in varying]
    if sizes[0] * sizes[1] != n:
        return list(range(n))
    if sizes[0] % 2:
        varying, sizes = varying[::-1], sizes[::-1]
        if sizes[0] % 2:
            return list(range(n))
    lows = [min(c[a] for c in coords) for a in varying]
    path = []
    for u in range(sizes[0]):
        span = range(1, sizes[1]) if u % 2 == 0 else range(sizes[1] - 1, 0, -1)
        path += [(u, v) for v in span]
    path += [(u, 0) for u in range(sizes[0] - 1, -1, -1)]
    order = []
    for u, v in path:
        key = list(coords[0])
        key[varying[0]] = lows[0] + u
        key[varying[1]] = lows[1] + v
        order.append(where[tuple(key)])
    return order


def gather_rows(block, axis):
    n = lax.axis_size(axis)
    if n & (n - 1):
        return lax.all_gather(block, axis, axis=0, tiled=True)
    me = lax.axis_index(axis)
    bit = 1
    while bit < n:
        pairs = [(i, i ^ bit) for i in range(n)]
        other = lax.ppermute(block, axis, pairs)
        low = (me & bit) == 0
        block = jnp.where(low, jnp.concatenate([block, other]), jnp.concatenate([other, block]))
        bit *= 2
    return block


def butterfly_sum(value, axis):
    n = lax.axis_size(axis)
    if n & (n - 1):
        return lax.psum(value, axis)
    bit = 1
    while bit < n:
        pairs = [(i, i ^ bit) for i in range(n)]
        value = value + lax.ppermute(value, axis, pairs)
        bit *= 2
    return value


def per_device(ring, expression, design, quantile_level):
    n = len(ring)
    width = design.shape[1]
    span = expression.shape[1] // n
    identity = jnp.eye(width, dtype=jnp.float32)
    design_all = gather_rows(design, "cell")
    sent = expression + (design_all[0, 0] * 0).astype(expression.dtype)
    expression_genes = lax.all_to_all(sent, "cell", 1, 0, tiled=True)
    gram_total = lax.dot_general(
        design_all, design_all, (((0,), (0,)), ((), ())), preferred_element_type=jnp.float32
    )
    inverse = invert(gram_total + identity)
    crossed = lax.dot_general(
        expression_genes, design_all, (((0,), (0,)), ((), ())), preferred_element_type=jnp.float32
    )
    coef = matmul(crossed, inverse)
    local_moment = lax.dot_general(
        coef, coef, (((0,), (0,)), ((), ())), precision=lax.Precision.HIGHEST
    )
    moment = butterfly_sum(butterfly_sum(local_moment, "gene"), "cell")
    root_inv = newton(moment)
    low_rank_coef = coef - shrink_rate / math.sqrt(width) * matmul(coef, root_inv)
    coef_low_t = coef.astype(jnp.bfloat16).T

    ring_arr = jnp.array(ring, dtype=jnp.int32)
    pos_arr = jnp.array([ring.index(i) for i in range(n)], dtype=jnp.int32)
    me = lax.axis_index("cell")
    pos = pos_arr[me]
    forward = [(ring[q], ring[(q + 1) % n]) for q in range(n)]
    backward = [(ring[(q + 1) % n], ring[q]) for q in range(n)]

    out = jnp.zeros(expression.shape, jnp.bfloat16)

    def place(out, block, owner):
        start = owner * span
        fitted = jnp.dot(design, block, preferred_element_type=jnp.float32)
        local = lax.dynamic_slice_in_dim(expression, start, span, axis=1).astype(jnp.float32)
        level = lax.dynamic_slice_in_dim(quantile_level, start, span)[None, :]
        slack = local - fitted
        piece = (slack - jnp.clip(slack, level - 1.0, level)).astype(jnp.bfloat16)
        return lax.dynamic_update_slice_in_dim(out, piece, start, axis=1)

    out = place(out, coef_low_t, me)
    ahead, behind = coef_low_t, coef_low_t
    for step in range(1, n // 2 + 1):
        ahead = lax.ppermute(ahead, "cell", forward)
        out = place(out, ahead, ring_arr[(pos - step) % n])
        if step <= (n - 1) // 2:
            behind = lax.ppermute(behind, "cell", backward)
            out = place(out, behind, ring_arr[(pos + step) % n])
    return (out, low_rank_coef)


def solution(mesh):
    placed = (P(("grp", "cell"), "gene"), P(("grp", "cell"), None), P("gene"))
    ring = cell_ring(mesh)
    return jax.shard_map(
        functools.partial(per_device, ring),
        mesh=mesh,
        in_specs=placed,
        out_specs=(P(("grp", "cell"), "gene"), P(("grp", "gene", "cell"), None)),
        check_vma=False,
    )
```

```python
import functools
import math

import jax
import jax.numpy as jnp
from jax import lax
from jax.sharding import PartitionSpec as P

NS_STEPS = 8


shrink_rate = 0.25


def matmul(left, right):
    return jnp.dot(left, right, precision=lax.Precision.HIGHEST)


def invert(matrix):
    identity = jnp.eye(matrix.shape[0], dtype=jnp.float32)
    factor = jnp.linalg.cholesky(matrix)
    lower_inv = lax.linalg.triangular_solve(factor, identity, left_side=True, lower=True)
    return matmul(lower_inv.T, lower_inv)


def newton(moment):
    identity = jnp.eye(moment.shape[0], dtype=jnp.float32)
    current = moment / jnp.trace(moment)
    root_inv = identity
    for sweep in range(NS_STEPS):
        middle = 1.5 * identity - 0.5 * matmul(root_inv, current)
        current = matmul(current, middle)
        root_inv = matmul(middle, root_inv)
    return root_inv


def cell_ring(mesh):
    devices = mesh.devices
    names = list(mesh.axis_names)
    index = [0] * len(names)
    index[names.index("cell")] = slice(None)
    line = list(devices[tuple(index)].reshape(-1))
    n = len(line)
    try:
        coords = [tuple(d.coords) for d in line]
    except (AttributeError, TypeError):
        return list(range(n))
    varying = [a for a in range(len(coords[0])) if len({c[a] for c in coords}) > 1]
    where = {c: i for i, c in enumerate(coords)}
    if len(varying) == 1:
        return sorted(range(n), key=lambda i: coords[i][varying[0]])
    if len(varying) != 2:
        return list(range(n))
    sizes = [len({c[a] for c in coords}) for a in varying]
    if sizes[0] * sizes[1] != n:
        return list(range(n))
    if sizes[0] % 2:
        varying, sizes = varying[::-1], sizes[::-1]
        if sizes[0] % 2:
            return list(range(n))
    lows = [min(c[a] for c in coords) for a in varying]
    path = []
    for u in range(sizes[0]):
        span = range(1, sizes[1]) if u % 2 == 0 else range(sizes[1] - 1, 0, -1)
        path += [(u, v) for v in span]
    path += [(u, 0) for u in range(sizes[0] - 1, -1, -1)]
    order = []
    for u, v in path:
        key = list(coords[0])
        key[varying[0]] = lows[0] + u
        key[varying[1]] = lows[1] + v
        order.append(where[tuple(key)])
    return order


def gather_blocks(block, axis):
    n = lax.axis_size(axis)
    me = lax.axis_index(axis)
    received = [block]
    for shift in range(1, n):
        pairs = [(i, (i + shift) % n) for i in range(n)]
        received.append(lax.ppermute(block, axis, pairs))
    stacked = jnp.stack(received)
    return jnp.take(stacked, (me - jnp.arange(n)) % n, axis=0)


def butterfly_sum(value, axis):
    n = lax.axis_size(axis)
    if n & (n - 1):
        return lax.psum(value, axis)
    bit = 1
    while bit < n:
        pairs = [(i, i ^ bit) for i in range(n)]
        value = value + lax.ppermute(value, axis, pairs)
        bit *= 2
    return value


def per_device(ring, expression, design, quantile_level):
    n = len(ring)
    width = design.shape[1]
    span = expression.shape[1] // n
    identity = jnp.eye(width, dtype=jnp.float32)
    design_all = gather_blocks(design, "cell").reshape(-1, width)
    sent = expression + (design_all[0, 0] * 0).astype(expression.dtype)
    expression_genes = lax.all_to_all(sent, "cell", 1, 0, tiled=True)
    gram_total = lax.dot_general(
        design_all, design_all, (((0,), (0,)), ((), ())), preferred_element_type=jnp.float32
    )
    inverse = invert(gram_total + identity)
    crossed = lax.dot_general(
        expression_genes, design_all, (((0,), (0,)), ((), ())), preferred_element_type=jnp.float32
    )
    coef = matmul(crossed, inverse)
    local_moment = lax.dot_general(
        coef, coef, (((0,), (0,)), ((), ())), precision=lax.Precision.HIGHEST
    )
    chip_moment = butterfly_sum(local_moment, "gene")
    moment = jnp.sum(gather_blocks(chip_moment, "cell"), axis=0)
    root_inv = newton(moment)
    low_rank_coef = coef - shrink_rate / math.sqrt(width) * matmul(coef, root_inv)
    coef_low_t = coef.astype(jnp.bfloat16).T

    ring_arr = jnp.array(ring, dtype=jnp.int32)
    pos_arr = jnp.array([ring.index(i) for i in range(n)], dtype=jnp.int32)
    me = lax.axis_index("cell")
    pos = pos_arr[me]
    forward = [(ring[q], ring[(q + 1) % n]) for q in range(n)]
    backward = [(ring[(q + 1) % n], ring[q]) for q in range(n)]

    out = jnp.zeros(expression.shape, jnp.bfloat16)

    def place(out, block, owner):
        start = owner * span
        fitted = jnp.dot(design, block, preferred_element_type=jnp.float32)
        local = lax.dynamic_slice_in_dim(expression, start, span, axis=1).astype(jnp.float32)
        level = lax.dynamic_slice_in_dim(quantile_level, start, span)[None, :]
        slack = local - fitted
        piece = (slack - jnp.clip(slack, level - 1.0, level)).astype(jnp.bfloat16)
        return lax.dynamic_update_slice_in_dim(out, piece, start, axis=1)

    out = place(out, coef_low_t, me)
    ahead, behind = coef_low_t, coef_low_t
    for step in range(1, n // 2 + 1):
        ahead = lax.ppermute(ahead, "cell", forward)
        out = place(out, ahead, ring_arr[(pos - step) % n])
        if step <= (n - 1) // 2:
            behind = lax.ppermute(behind, "cell", backward)
            out = place(out, behind, ring_arr[(pos + step) % n])
    return (out, low_rank_coef)


def solution(mesh):
    placed = (P(("grp", "cell"), "gene"), P(("grp", "cell"), None), P("gene"))
    ring = cell_ring(mesh)
    return jax.shard_map(
        functools.partial(per_device, ring),
        mesh=mesh,
        in_specs=placed,
        out_specs=(P(("grp", "cell"), "gene"), P(("grp", "gene", "cell"), None)),
        check_vma=False,
    )
```

```python
import functools
import math

import jax
import jax.numpy as jnp
from jax import lax
from jax.sharding import PartitionSpec as P
from jax.experimental import pallas as pl
from jax.experimental.pallas import tpu as pltpu

NS_STEPS = 8


shrink_rate = 0.25


def matmul(left, right):
    return jnp.dot(left, right, precision=lax.Precision.HIGHEST)


def invert(matrix):
    identity = jnp.eye(matrix.shape[0], dtype=jnp.float32)
    factor = jnp.linalg.cholesky(matrix)
    lower_inv = lax.linalg.triangular_solve(factor, identity, left_side=True, lower=True)
    return matmul(lower_inv.T, lower_inv)


def newton(moment):
    identity = jnp.eye(moment.shape[0], dtype=jnp.float32)
    current = moment / jnp.trace(moment)
    root_inv = identity
    for sweep in range(NS_STEPS):
        middle = 1.5 * identity - 0.5 * matmul(root_inv, current)
        current = matmul(current, middle)
        root_inv = matmul(middle, root_inv)
    return root_inv


def cell_ring(mesh):
    devices = mesh.devices
    names = list(mesh.axis_names)
    index = [0] * len(names)
    index[names.index("cell")] = slice(None)
    line = list(devices[tuple(index)].reshape(-1))
    n = len(line)
    try:
        coords = [tuple(d.coords) for d in line]
    except (AttributeError, TypeError):
        return list(range(n))
    varying = [a for a in range(len(coords[0])) if len({c[a] for c in coords}) > 1]
    where = {c: i for i, c in enumerate(coords)}
    if len(varying) == 1:
        return sorted(range(n), key=lambda i: coords[i][varying[0]])
    if len(varying) != 2:
        return list(range(n))
    sizes = [len({c[a] for c in coords}) for a in varying]
    if sizes[0] * sizes[1] != n:
        return list(range(n))
    if sizes[0] % 2:
        varying, sizes = varying[::-1], sizes[::-1]
        if sizes[0] % 2:
            return list(range(n))
    lows = [min(c[a] for c in coords) for a in varying]
    path = []
    for u in range(sizes[0]):
        span = range(1, sizes[1]) if u % 2 == 0 else range(sizes[1] - 1, 0, -1)
        path += [(u, v) for v in span]
    path += [(u, 0) for u in range(sizes[0] - 1, -1, -1)]
    order = []
    for u, v in path:
        key = list(coords[0])
        key[varying[0]] = lows[0] + u
        key[varying[1]] = lows[1] + v
        order.append(where[tuple(key)])
    return order


def gather_rows(block, axis):
    n = lax.axis_size(axis)
    if n & (n - 1):
        return lax.all_gather(block, axis, axis=0, tiled=True)
    me = lax.axis_index(axis)
    bit = 1
    while bit < n:
        pairs = [(i, i ^ bit) for i in range(n)]
        other = lax.ppermute(block, axis, pairs)
        low = (me & bit) == 0
        block = jnp.where(low, jnp.concatenate([block, other]), jnp.concatenate([other, block]))
        bit *= 2
    return block


def butterfly_sum(value, axis):
    n = lax.axis_size(axis)
    if n & (n - 1):
        return lax.psum(value, axis)
    bit = 1
    while bit < n:
        pairs = [(i, i ^ bit) for i in range(n)]
        value = value + lax.ppermute(value, axis, pairs)
        bit *= 2
    return value


def place_kernel(owner_ref, design_ref, level_ref, expression_ref, *rest):
    block_refs, out_ref = rest[:-1], rest[-1]
    span = block_refs[0].shape[1]
    design = design_ref[...]
    for slot, block_ref in enumerate(block_refs):
        start = pl.multiple_of(owner_ref[slot] * span, span)
        columns = pl.ds(start, span)
        fitted = jnp.dot(design, block_ref[...], preferred_element_type=jnp.float32)
        slack = expression_ref[:, columns].astype(jnp.float32) - fitted
        level = level_ref[:, columns]
        out_ref[:, columns] = (slack - jnp.clip(slack, level - 1.0, level)).astype(out_ref.dtype)


def place_blocks(design, blocks, owners, expression, quantile_level):
    span = blocks[0].shape[1]
    level = quantile_level.reshape(1, -1)
    if span % 128:
        out = jnp.zeros(expression.shape, jnp.bfloat16)
        for slot, block in enumerate(blocks):
            start = owners[slot] * span
            fitted = jnp.dot(design, block, preferred_element_type=jnp.float32)
            local = lax.dynamic_slice_in_dim(expression, start, span, axis=1).astype(jnp.float32)
            part = lax.dynamic_slice_in_dim(level, start, span, axis=1)
            slack = local - fitted
            piece = (slack - jnp.clip(slack, part - 1.0, part)).astype(jnp.bfloat16)
            out = lax.dynamic_update_slice_in_dim(out, piece, start, axis=1)
        return out
    vmem = pl.BlockSpec(memory_space=pltpu.VMEM)
    return pl.pallas_call(
        place_kernel,
        out_shape=jax.ShapeDtypeStruct(expression.shape, jnp.bfloat16),
        in_specs=[pl.BlockSpec(memory_space=pltpu.SMEM)] + [vmem] * (3 + len(blocks)),
        out_specs=vmem,
        compiler_params=pltpu.CompilerParams(vmem_limit_bytes=48 * 1024 * 1024),
    )(owners, design, level, expression, *blocks)


def per_device(ring, expression, design, quantile_level):
    n = len(ring)
    width = design.shape[1]
    span = expression.shape[1] // n
    identity = jnp.eye(width, dtype=jnp.float32)
    design_all = gather_rows(design, "cell")
    sent = expression + (design_all[0, 0] * 0).astype(expression.dtype)
    expression_genes = lax.all_to_all(sent, "cell", 1, 0, tiled=True)
    gram_total = lax.dot_general(
        design_all, design_all, (((0,), (0,)), ((), ())), preferred_element_type=jnp.float32
    )
    inverse = invert(gram_total + identity)
    crossed = lax.dot_general(
        expression_genes, design_all, (((0,), (0,)), ((), ())), preferred_element_type=jnp.float32
    )
    coef = matmul(crossed, inverse)
    local_moment = lax.dot_general(
        coef, coef, (((0,), (0,)), ((), ())), precision=lax.Precision.HIGHEST
    )
    moment = butterfly_sum(butterfly_sum(local_moment, "gene"), "cell")
    root_inv = newton(moment)
    low_rank_coef = coef - shrink_rate / math.sqrt(width) * matmul(coef, root_inv)
    coef_low_t = coef.astype(jnp.bfloat16).T

    ring_arr = jnp.array(ring, dtype=jnp.int32)
    pos_arr = jnp.array([ring.index(i) for i in range(n)], dtype=jnp.int32)
    me = lax.axis_index("cell")
    pos = pos_arr[me]
    forward = [(ring[q], ring[(q + 1) % n]) for q in range(n)]
    backward = [(ring[(q + 1) % n], ring[q]) for q in range(n)]

    blocks = [coef_low_t]
    owners = [me]
    ahead, behind = coef_low_t, coef_low_t
    for step in range(1, n // 2 + 1):
        ahead = lax.ppermute(ahead, "cell", forward)
        blocks.append(ahead)
        owners.append(ring_arr[(pos - step) % n])
        if step <= (n - 1) // 2:
            behind = lax.ppermute(behind, "cell", backward)
            blocks.append(behind)
            owners.append(ring_arr[(pos + step) % n])
    out = place_blocks(design, blocks, jnp.stack(owners).astype(jnp.int32), expression, quantile_level)
    return (out, low_rank_coef)


def solution(mesh):
    placed = (P(("grp", "cell"), "gene"), P(("grp", "cell"), None), P("gene"))
    ring = cell_ring(mesh)
    return jax.shard_map(
        functools.partial(per_device, ring),
        mesh=mesh,
        in_specs=placed,
        out_specs=(P(("grp", "cell"), "gene"), P(("grp", "gene", "cell"), None)),
        check_vma=False,
    )
```

```python
import functools
import math

import jax
import jax.numpy as jnp
from jax import lax
from jax.sharding import PartitionSpec as P
from jax.experimental import pallas as pl
from jax.experimental.pallas import tpu as pltpu

NS_STEPS = 8


shrink_rate = 0.25


def matmul(left, right):
    return jnp.dot(left, right, precision=lax.Precision.HIGHEST)


def invert(matrix):
    identity = jnp.eye(matrix.shape[0], dtype=jnp.float32)
    factor = jnp.linalg.cholesky(matrix)
    lower_inv = lax.linalg.triangular_solve(factor, identity, left_side=True, lower=True)
    return matmul(lower_inv.T, lower_inv)


def newton(moment):
    identity = jnp.eye(moment.shape[0], dtype=jnp.float32)
    current = moment / jnp.trace(moment)
    root_inv = identity
    for sweep in range(NS_STEPS):
        middle = 1.5 * identity - 0.5 * matmul(root_inv, current)
        current = matmul(current, middle)
        root_inv = matmul(middle, root_inv)
    return root_inv


def cell_ring(mesh):
    devices = mesh.devices
    names = list(mesh.axis_names)
    index = [0] * len(names)
    index[names.index("cell")] = slice(None)
    line = list(devices[tuple(index)].reshape(-1))
    n = len(line)
    try:
        coords = [tuple(d.coords) for d in line]
    except (AttributeError, TypeError):
        return list(range(n))
    varying = [a for a in range(len(coords[0])) if len({c[a] for c in coords}) > 1]
    where = {c: i for i, c in enumerate(coords)}
    if len(varying) == 1:
        return sorted(range(n), key=lambda i: coords[i][varying[0]])
    if len(varying) != 2:
        return list(range(n))
    sizes = [len({c[a] for c in coords}) for a in varying]
    if sizes[0] * sizes[1] != n:
        return list(range(n))
    if sizes[0] % 2:
        varying, sizes = varying[::-1], sizes[::-1]
        if sizes[0] % 2:
            return list(range(n))
    lows = [min(c[a] for c in coords) for a in varying]
    path = []
    for u in range(sizes[0]):
        span = range(1, sizes[1]) if u % 2 == 0 else range(sizes[1] - 1, 0, -1)
        path += [(u, v) for v in span]
    path += [(u, 0) for u in range(sizes[0] - 1, -1, -1)]
    order = []
    for u, v in path:
        key = list(coords[0])
        key[varying[0]] = lows[0] + u
        key[varying[1]] = lows[1] + v
        order.append(where[tuple(key)])
    return order


def gather_rows(block, axis):
    n = lax.axis_size(axis)
    if n & (n - 1):
        return lax.all_gather(block, axis, axis=0, tiled=True)
    me = lax.axis_index(axis)
    bit = 1
    while bit < n:
        pairs = [(i, i ^ bit) for i in range(n)]
        other = lax.ppermute(block, axis, pairs)
        low = (me & bit) == 0
        block = jnp.where(low, jnp.concatenate([block, other]), jnp.concatenate([other, block]))
        bit *= 2
    return block


def butterfly_sum(value, axis):
    n = lax.axis_size(axis)
    if n & (n - 1):
        return lax.psum(value, axis)
    bit = 1
    while bit < n:
        pairs = [(i, i ^ bit) for i in range(n)]
        value = value + lax.ppermute(value, axis, pairs)
        bit *= 2
    return value


def place_kernel(owner_ref, design_ref, level_ref, expression_ref, *rest):
    block_refs, out_ref = rest[:-1], rest[-1]
    span = block_refs[0].shape[1]
    design = design_ref[...]
    for slot, block_ref in enumerate(block_refs):
        start = pl.multiple_of(owner_ref[slot] * span, span)
        columns = pl.ds(start, span)
        fitted = jnp.dot(design, block_ref[...], preferred_element_type=jnp.float32)
        slack = expression_ref[:, columns].astype(jnp.float32) - fitted
        level = level_ref[:, columns]
        out_ref[:, columns] = (slack - jnp.clip(slack, level - 1.0, level)).astype(out_ref.dtype)


def place_blocks(design, blocks, owners, expression, quantile_level):
    span = blocks[0].shape[1]
    level = quantile_level.reshape(1, -1)
    if span % 128:
        out = jnp.zeros(expression.shape, jnp.bfloat16)
        for slot, block in enumerate(blocks):
            start = owners[slot] * span
            fitted = jnp.dot(design, block, preferred_element_type=jnp.float32)
            local = lax.dynamic_slice_in_dim(expression, start, span, axis=1).astype(jnp.float32)
            part = lax.dynamic_slice_in_dim(level, start, span, axis=1)
            slack = local - fitted
            piece = (slack - jnp.clip(slack, part - 1.0, part)).astype(jnp.bfloat16)
            out = lax.dynamic_update_slice_in_dim(out, piece, start, axis=1)
        return out
    vmem = pl.BlockSpec(memory_space=pltpu.VMEM)
    return pl.pallas_call(
        place_kernel,
        out_shape=jax.ShapeDtypeStruct(expression.shape, jnp.bfloat16),
        in_specs=[pl.BlockSpec(memory_space=pltpu.SMEM)] + [vmem] * (3 + len(blocks)),
        out_specs=vmem,
        compiler_params=pltpu.CompilerParams(vmem_limit_bytes=48 * 1024 * 1024),
    )(owners, design, level, expression, *blocks)


def per_device(ring, expression, design, quantile_level):
    n = len(ring)
    width = design.shape[1]
    span = expression.shape[1] // n
    identity = jnp.eye(width, dtype=jnp.float32)
    design_all = gather_rows(design, "cell")
    sent = expression + (design_all[0, 0] * 0).astype(expression.dtype)
    expression_genes = lax.all_to_all(sent, "cell", 1, 0, tiled=True)
    gram_total = lax.dot_general(
        design_all, design_all, (((0,), (0,)), ((), ())), preferred_element_type=jnp.float32
    )
    inverse = invert(gram_total + identity)
    crossed = lax.dot_general(
        expression_genes, design_all, (((0,), (0,)), ((), ())), preferred_element_type=jnp.float32
    )
    coef = matmul(crossed, inverse)
    local_moment = lax.dot_general(
        coef, coef, (((0,), (0,)), ((), ())), precision=lax.Precision.HIGHEST
    )
    chip_moment = butterfly_sum(local_moment, "gene")
    coef_low_t = coef.astype(jnp.bfloat16).T

    ring_arr = jnp.array(ring, dtype=jnp.int32)
    pos_arr = jnp.array([ring.index(i) for i in range(n)], dtype=jnp.int32)
    me = lax.axis_index("cell")
    pos = pos_arr[me]
    forward = [(ring[q], ring[(q + 1) % n]) for q in range(n)]
    backward = [(ring[(q + 1) % n], ring[q]) for q in range(n)]

    blocks, moments = [coef_low_t], [chip_moment]
    owners = [me]
    ahead = behind = (coef_low_t, chip_moment)
    for step in range(1, n // 2 + 1):
        ahead = lax.ppermute(ahead, "cell", forward)
        blocks.append(ahead[0])
        moments.append(ahead[1])
        owners.append(ring_arr[(pos - step) % n])
        if step <= (n - 1) // 2:
            behind = lax.ppermute(behind, "cell", backward)
            blocks.append(behind[0])
            moments.append(behind[1])
            owners.append(ring_arr[(pos + step) % n])
    owners = jnp.stack(owners).astype(jnp.int32)
    slots = jnp.zeros((n,), jnp.int32).at[owners].set(jnp.arange(n, dtype=jnp.int32))
    moment = jnp.sum(jnp.take(jnp.stack(moments), slots, axis=0), axis=0)
    root_inv = newton(moment)
    low_rank_coef = coef - shrink_rate / math.sqrt(width) * matmul(coef, root_inv)
    out = place_blocks(design, blocks, owners, expression, quantile_level)
    return (out, low_rank_coef)


def solution(mesh):
    placed = (P(("grp", "cell"), "gene"), P(("grp", "cell"), None), P("gene"))
    ring = cell_ring(mesh)
    return jax.shard_map(
        functools.partial(per_device, ring),
        mesh=mesh,
        in_specs=placed,
        out_specs=(P(("grp", "cell"), "gene"), P(("grp", "gene", "cell"), None)),
        check_vma=False,
    )
```

```python
import functools
import math

import jax
import jax.numpy as jnp
from jax import lax
from jax.sharding import PartitionSpec as P
from jax.experimental import pallas as pl
from jax.experimental.pallas import tpu as pltpu

NS_STEPS = 8


shrink_rate = 0.25


def matmul(left, right):
    return jnp.dot(left, right, precision=lax.Precision.HIGHEST)


def invert(matrix):
    identity = jnp.eye(matrix.shape[0], dtype=jnp.float32)
    factor = jnp.linalg.cholesky(matrix)
    lower_inv = lax.linalg.triangular_solve(factor, identity, left_side=True, lower=True)
    return matmul(lower_inv.T, lower_inv)


def newton(moment):
    identity = jnp.eye(moment.shape[0], dtype=jnp.float32)
    current = moment / jnp.trace(moment)
    root_inv = identity
    for sweep in range(NS_STEPS):
        middle = 1.5 * identity - 0.5 * matmul(root_inv, current)
        current = matmul(current, middle)
        root_inv = matmul(middle, root_inv)
    return root_inv


def cell_ring(mesh):
    devices = mesh.devices
    names = list(mesh.axis_names)
    index = [0] * len(names)
    index[names.index("cell")] = slice(None)
    line = list(devices[tuple(index)].reshape(-1))
    n = len(line)
    try:
        coords = [tuple(d.coords) for d in line]
    except (AttributeError, TypeError):
        return list(range(n))
    varying = [a for a in range(len(coords[0])) if len({c[a] for c in coords}) > 1]
    where = {c: i for i, c in enumerate(coords)}
    if len(varying) == 1:
        return sorted(range(n), key=lambda i: coords[i][varying[0]])
    if len(varying) != 2:
        return list(range(n))
    sizes = [len({c[a] for c in coords}) for a in varying]
    if sizes[0] * sizes[1] != n:
        return list(range(n))
    if sizes[0] % 2:
        varying, sizes = varying[::-1], sizes[::-1]
        if sizes[0] % 2:
            return list(range(n))
    lows = [min(c[a] for c in coords) for a in varying]
    path = []
    for u in range(sizes[0]):
        span = range(1, sizes[1]) if u % 2 == 0 else range(sizes[1] - 1, 0, -1)
        path += [(u, v) for v in span]
    path += [(u, 0) for u in range(sizes[0] - 1, -1, -1)]
    order = []
    for u, v in path:
        key = list(coords[0])
        key[varying[0]] = lows[0] + u
        key[varying[1]] = lows[1] + v
        order.append(where[tuple(key)])
    return order


def gather_rows(block, axis):
    n = lax.axis_size(axis)
    if n & (n - 1):
        return lax.all_gather(block, axis, axis=0, tiled=True)
    me = lax.axis_index(axis)
    bit = 1
    while bit < n:
        pairs = [(i, i ^ bit) for i in range(n)]
        other = lax.ppermute(block, axis, pairs)
        low = (me & bit) == 0
        block = jnp.where(low, jnp.concatenate([block, other]), jnp.concatenate([other, block]))
        bit *= 2
    return block


def butterfly_sum(value, axis):
    n = lax.axis_size(axis)
    if n & (n - 1):
        return lax.psum(value, axis)
    bit = 1
    while bit < n:
        pairs = [(i, i ^ bit) for i in range(n)]
        value = value + lax.ppermute(value, axis, pairs)
        bit *= 2
    return value


def lookup(table, index):
    value = jnp.int32(table[0])
    for entry, item in enumerate(table[1:], 1):
        value = jnp.where(index == entry, jnp.int32(item), value)
    return value


def place_kernel(ring, shifts, design_ref, level_ref, expression_ref, *rest):
    block_refs, out_ref = rest[:-1], rest[-1]
    n = len(ring)
    span = block_refs[0].shape[1]
    pos = lookup([ring.index(i) for i in range(n)], lax.axis_index("cell"))
    design = design_ref[...]
    for shift, block_ref in zip(shifts, block_refs):
        owner = lookup(ring, (pos + shift + n) % n)
        start = pl.multiple_of(owner * span, span)
        columns = pl.ds(start, span)
        fitted = jnp.dot(design, block_ref[...], preferred_element_type=jnp.float32)
        slack = expression_ref[:, columns].astype(jnp.float32) - fitted
        level = level_ref[:, columns]
        out_ref[:, columns] = (slack - jnp.clip(slack, level - 1.0, level)).astype(out_ref.dtype)


def place_blocks(ring, shifts, design, blocks, owners, expression, quantile_level):
    span = blocks[0].shape[1]
    level = quantile_level.reshape(1, -1)
    if span % 128:
        out = jnp.zeros(expression.shape, jnp.bfloat16)
        for slot, block in enumerate(blocks):
            start = owners[slot] * span
            fitted = jnp.dot(design, block, preferred_element_type=jnp.float32)
            local = lax.dynamic_slice_in_dim(expression, start, span, axis=1).astype(jnp.float32)
            part = lax.dynamic_slice_in_dim(level, start, span, axis=1)
            slack = local - fitted
            piece = (slack - jnp.clip(slack, part - 1.0, part)).astype(jnp.bfloat16)
            out = lax.dynamic_update_slice_in_dim(out, piece, start, axis=1)
        return out
    vmem = pl.BlockSpec(memory_space=pltpu.VMEM)
    return pl.pallas_call(
        functools.partial(place_kernel, ring, shifts),
        out_shape=jax.ShapeDtypeStruct(expression.shape, jnp.bfloat16),
        in_specs=[vmem] * (3 + len(blocks)),
        out_specs=vmem,
        compiler_params=pltpu.CompilerParams(vmem_limit_bytes=48 * 1024 * 1024),
    )(design, level, expression, *blocks)


def per_device(ring, expression, design, quantile_level):
    n = len(ring)
    width = design.shape[1]
    span = expression.shape[1] // n
    identity = jnp.eye(width, dtype=jnp.float32)
    design_all = gather_rows(design, "cell")
    sent = expression + (design_all[0, 0] * 0).astype(expression.dtype)
    expression_genes = lax.all_to_all(sent, "cell", 1, 0, tiled=True)
    gram_total = lax.dot_general(
        design_all, design_all, (((0,), (0,)), ((), ())), preferred_element_type=jnp.float32
    )
    inverse = invert(gram_total + identity)
    crossed = lax.dot_general(
        expression_genes, design_all, (((0,), (0,)), ((), ())), preferred_element_type=jnp.float32
    )
    coef = matmul(crossed, inverse)
    local_moment = lax.dot_general(
        coef, coef, (((0,), (0,)), ((), ())), precision=lax.Precision.HIGHEST
    )
    chip_moment = butterfly_sum(local_moment, "gene")
    coef_low_t = coef.astype(jnp.bfloat16).T

    ring_arr = jnp.array(ring, dtype=jnp.int32)
    pos_arr = jnp.array([ring.index(i) for i in range(n)], dtype=jnp.int32)
    me = lax.axis_index("cell")
    pos = pos_arr[me]
    forward = [(ring[q], ring[(q + 1) % n]) for q in range(n)]
    backward = [(ring[(q + 1) % n], ring[q]) for q in range(n)]

    blocks, moments = [coef_low_t], [chip_moment]
    owners, shifts = [me], [0]

    def tie(block, moment):
        block = block + (moment[0, 0] * 0).astype(block.dtype)
        moment = moment + (block[0, 0] * 0).astype(moment.dtype)
        return block, moment

    ahead = behind = (coef_low_t, chip_moment)
    for step in range(1, n // 2 + 1):
        ahead = tuple(lax.ppermute(tie(*ahead), "cell", forward))
        blocks.append(ahead[0])
        moments.append(ahead[1])
        owners.append(ring_arr[(pos - step) % n])
        shifts.append(-step)
        if step <= (n - 1) // 2:
            behind = tuple(lax.ppermute(tie(*behind), "cell", backward))
            blocks.append(behind[0])
            moments.append(behind[1])
            owners.append(ring_arr[(pos + step) % n])
            shifts.append(step)
    owners = jnp.stack(owners).astype(jnp.int32)
    slots = jnp.zeros((n,), jnp.int32).at[owners].set(jnp.arange(n, dtype=jnp.int32))
    moment = jnp.sum(jnp.take(jnp.stack(moments), slots, axis=0), axis=0)
    root_inv = newton(moment)
    low_rank_coef = coef - shrink_rate / math.sqrt(width) * matmul(coef, root_inv)
    out = place_blocks(ring, shifts, design, blocks, owners, expression, quantile_level)
    return (out, low_rank_coef)


def solution(mesh):
    placed = (P(("grp", "cell"), "gene"), P(("grp", "cell"), None), P("gene"))
    ring = cell_ring(mesh)
    return jax.shard_map(
        functools.partial(per_device, ring),
        mesh=mesh,
        in_specs=placed,
        out_specs=(P(("grp", "cell"), "gene"), P(("grp", "gene", "cell"), None)),
        check_vma=False,
    )
```
